256 devices in a mesh: row: 8 (over z), col: 32 (over y, x, core).
Axes of the slice: x: 4, y: 4, z: 8, core: 2. Of those that a mesh axis runs over, the one named last changes fastest.
Arguments:
- hidden_in: bfloat16 [1024, 2304], P('row', 'col'), may hold values from -40 to 40
- attn_gain: float32 [2304], P('col'), may hold values from 0.1 to 1.9
- qkv_weight: bfloat16 [2304, 6912], P('col'), may hold values from -0.125 to 0.125
- out_weight: bfloat16 [2304, 2304], P(None, 'col'), may hold values from -0.125 to 0.125
- moe_gain: float32 [2304], P('col'), may hold values from 0.1 to 1.9
- router_weight: float32 [2304, 8], P('col'), may hold values from -0.125 to 0.125
- expert_gate: bfloat16 [8, 2304, 5760], P('row', None, 'col'), may hold values from -0.125 to 0.125
- expert_up: bfloat16 [8, 2304, 5760], P('row', None, 'col'), may hold values from -0.125 to 0.125
- expert_down: bfloat16 [8, 5760, 2304], P('row', 'col'), may hold values from -0.078125 to 0.078125
- cache_keys: bfloat16 [2048, 64, 2304], P(('row', 'col')), may hold values from -400 to 400
- cache_values: bfloat16 [2048, 64, 2304], P(('row', 'col')), may hold values from -12 to 12
- block_table: int32 [8, 4, 64], P('row'), may hold values from 0 to 2047, as said below
- prefix_lengths: int32 [8, 4], P('row'), may hold values from 1024 to 4096, as said below
- prompt_lengths: int32 [8, 4], P('row'), may hold values from 1 to 64, 128 in all within a row
- routed_experts: int32 [1024, 2], P('row'), may hold values from 0 to 7, all different within a row; in each aligned block of 128 rows (0 to 127, 128 to 255, ...) at most 64 rows name the same one
Outputs:
- attn_out: bfloat16 [1024, 2304], P('row', 'col')
- moe_out: bfloat16 [1024, 2304], P('row', 'col')
- layer_out: bfloat16 [1024, 2304], P('row', 'col')
The draws below stay inside these ranges and needn't reach their ends.
Inputs may be any that keep to these rules, and one draw needn't show every extreme that they name: `block_table`: entry [g, q, j] lies among the 8 pages that begin at (g * 32 + j % 32) * 8; the entries that fall among the same 8 pages are distinct. `prefix_lengths`: some request has exactly 4096 cached tokens. `prompt_lengths`: the 4 lengths of a group sum to 128; the longest of each group is exactly 64. `routed_experts`: the 2 experts of a token differ; among the tokens of one group no expert is named more than 64 times, and in some group an expert reaches 64; every expert is named by some token.
All inputs are finite; a program needn't handle non-finite values.
Results may differ from the reference program's by a relative error of at most 0.02.
The reference program's roundings to bfloat16 on the way count: a program that leaves them out, or rounds other values in their place, can miss the bound.
Values may be sent and summed in bfloat16 or wider, within the bound.
No kernel may reach another device: no remote copies, remote signals or barrier semaphores. Data moves between devices by JAX's collectives and lax.ppermute only.
A program may use at most 192 MiB of HBM per device.

```python
import math
import jax
import jax.numpy as jnp
import numpy as np
from jax import lax

D = 2304
HEADS = 36
HEAD_DIM = 64
FF = 5760
TOP = 2
TOK_ROW = 128
REQ_ROW = 4
PAGE = 64
PG_DEV = 2
SHARDS = 32
GROUPS = 8
TOKENS = 1024
HD = 2304
EXPERTS = 8
CAP = 64
MAXP = 64
POOL = 8
PAGES_ALL = 2048
MOST_LEN = 64


def draw_hidden_in(key, part):
    subkeys = jax.random.split(key, 3)
    feature = jnp.arange(D, dtype=jnp.float32) / D
    base_draw = jax.random.normal(subkeys[0], (TOKENS, D), jnp.float32)
    row_factor = jnp.exp(jax.random.uniform(subkeys[1], (TOKENS, 1), jnp.float32, math.log(0.4), math.log(4.0)))
    col_factor = jnp.exp(jax.random.uniform(subkeys[2], (1, D), jnp.float32, math.log(0.6), math.log(1.6)) + feature[None, :] * (math.log(3.0) / 2.0))
    values = base_draw * row_factor * col_factor
    return jnp.clip(values, -40.0, 40.0).astype(jnp.bfloat16)


def draw_cache_keys(key, part):
    subkeys = jax.random.split(key, 1)
    values = jax.random.normal(subkeys[0], (PAGES_ALL, PAGE, HD), jnp.float32)
    return jnp.clip(values, -400.0, 400.0).astype(jnp.bfloat16)


def draw_prefix_lengths(key, part):
    subkeys = jax.random.split(key, 2)
    longest = MAXP * PAGE
    values = jax.random.randint(subkeys[0], (GROUPS * REQ_ROW,), longest // 4, longest + 1)
    chosen_entry = jax.random.randint(subkeys[1], (), 0, GROUPS * REQ_ROW)
    flattened = jnp.where(jnp.arange(GROUPS * REQ_ROW) == chosen_entry, longest, values)
    return flattened.reshape(GROUPS, REQ_ROW).astype(jnp.int32)


def permute_pool(subkey):
    return jax.random.permutation(subkey, POOL)


def draw_block_table(key, part):
    col_blocks = MAXP // PG_DEV
    block_total = GROUPS * col_blocks
    subkeys = jax.random.split(key, block_total)
    permuted = jax.vmap(permute_pool)(subkeys)
    group_ids = jnp.arange(GROUPS)[:, None, None]
    request_ids = jnp.arange(REQ_ROW)[None, :, None]
    logical = jnp.arange(MAXP)[None, None, :]
    block_ids = group_ids * col_blocks + logical % col_blocks
    local_slot = permuted[block_ids, request_ids * PG_DEV + logical // col_blocks]
    return (block_ids * POOL + local_slot).astype(jnp.int32)


def block_scale(key, dims, cuts, least, top_value):
    def one(dim, shards_of):
        heights = jax.random.uniform(jax.random.fold_in(jax.random.fold_in(key, 6), dim), (shards_of,), jnp.float32, least / len(cuts), top_value / len(cuts))
        return jnp.repeat(jnp.exp(heights), dims[dim] // shards_of).reshape((-1,) + (1,) * (len(dims) - dim - 1))

    factor_of = one(*cuts[0])
    for cut in cuts[1:]:
        factor_of = factor_of * one(*cut)
    return factor_of


def split_up(count, total, most, slope):
    weights = [(1 << 20) // math.isqrt(grade ** slope) + 1 for grade in range(2, count + 1)]
    surplus, counts = total - most - (count - 1), [1] * (count - 1)
    while surplus > 0:
        movable = [i for i in range(count - 1) if counts[i] < most]
        pool, budget = sum([weights[i] for i in movable]), surplus
        for i in movable:
            extra = min(most - counts[i], max(1, budget * weights[i] // pool), surplus)
            counts[i] = counts[i] + extra
            surplus = surplus - extra
    return np.array([most] + counts)


def ragged(rng, amount, total, bound, slope):
    if amount == 2:
        one = jax.random.randint(rng, (), max(1, total - bound), min(bound, total - 1) + 1)
        return jnp.stack([one, total - one])
    lengths = jnp.asarray(split_up(amount, total, bound, slope), jnp.int32)
    pairs = (amount - 1) // 2
    source_of, taker = lengths[1:1 + 2 * pairs:2], lengths[2:2 + 2 * pairs:2]
    slack = jnp.minimum(source_of - 1, bound - taker)
    passed = jax.random.randint(jax.random.fold_in(rng, 1), (pairs,), 0, 1 << 20) % (slack + 1)
    lengths = lengths.at[1:1 + 2 * pairs:2].set(source_of - passed).at[2:2 + 2 * pairs:2].set(taker + passed)
    return lengths[jax.random.permutation(jax.random.fold_in(rng, 2), amount)]


def shared_out(stream_key, own, number, rows, amount, top, limit, skew):
    sequence = jax.random.permutation(stream_key, amount)
    heavy_load, ordinary = shares(amount, rows * top, limit, skew, True), shares(amount, rows * top, limit, skew, False)
    places = jnp.arange(amount)

    def named(sizes, rotation):
        used = int((sizes > 0).sum())
        fixed = max(1, used // 4)
        passed = fixed + (places - fixed + rotation * (used - fixed)) % max(1, amount - fixed)
        return jnp.zeros((amount,), jnp.int32).at[sequence[jnp.where(places < fixed, places, passed)]].set(jnp.asarray(sizes, jnp.int32))

    sizes = jnp.where(number % 4 == 0, named(heavy_load, number // 4), named(ordinary, number - number // 4 - 1))
    mixed = jax.random.permutation(jax.random.fold_in(own, 3), amount)
    source_of, taker = mixed[0:amount // 2 * 2:2], mixed[1:amount // 2 * 2:2]
    slack = jnp.minimum(sizes[source_of] - 1, limit - sizes[taker]) // 2
    slack = jnp.where((source_of == sequence[0]) | (taker == sequence[0]) | (sizes[taker] == 0), 0, jnp.maximum(slack, 0))
    passed = jax.random.randint(jax.random.fold_in(own, 4), (amount // 2,), 0, 1 << 20) % (slack + 1)
    sizes = sizes.at[source_of].add(-passed).at[taker].add(passed)
    items = jnp.searchsorted(jnp.cumsum(sizes), jnp.arange(rows * top), side="right").astype(jnp.int32)
    table = items.reshape(top, rows).T
    table = table[jax.random.permutation(jax.random.fold_in(own, 1), rows)]
    rotation = jax.random.randint(jax.random.fold_in(own, 2), (rows, 1), 0, top)
    return jnp.take_along_axis(table, (jnp.arange(top)[None, :] + rotation) % top, axis=1)


def shares(amount, total, most, lean, full):
    weights = [(1 << 20) // math.isqrt(rank ** lean) + 1 for rank in range(1, amount + 1)]
    largest = most if full else min(most, max(-(-total // amount), total * weights[0] // sum(weights)))
    least = 1 if total - largest >= amount - 1 else 0
    given, surplus = [largest] + [least] * (amount - 1), total - largest - least * (amount - 1)
    while surplus > 0:
        free = [i for i in range(1, amount) if given[i] < largest] or [i for i in range(1, amount) if given[i] < most]
        whole, remaining = sum([weights[i] for i in free]), surplus
        for i in free:
            extra = min(most - given[i], max(1, remaining * weights[i] // whole), surplus)
            given[i] = given[i] + extra
            surplus = surplus - extra
    return np.array(given)


def normal_values(key, dims, scale, reach, cuts=(), kind=jnp.bfloat16):
    gain = block_scale(key, dims, cuts, -0.22, 0.18) if cuts else 1.0
    array = jax.random.normal(key, dims, jnp.float32) * scale * gain
    return jnp.minimum(jnp.maximum(array, -reach), reach).astype(kind)


def setup_inputs(seed: int = 0) -> dict:
    key_of = jax.random.split(jax.random.key(seed), 16)
    hidden_in = draw_hidden_in(jax.random.fold_in(key_of[15], 71), 0)
    attn_gain = jnp.clip(1.0 + 0.18 * jax.random.normal(key_of[1], (D,), jnp.float32), 0.1, 1.9)
    qkv_weight = normal_values(key_of[2], (D, 3 * HD), D ** -0.5, 0.125, ((0, 32),))
    out_weight = normal_values(key_of[3], (HD, D), HD ** -0.5, 0.125, ((1, 32),))
    moe_gain = jnp.clip(1.0 + 0.18 * jax.random.normal(key_of[4], (D,), jnp.float32), 0.1, 1.9)
    router_weight = normal_values(key_of[5], (D, EXPERTS), D ** -0.5, 0.125, ((0, 32),), jnp.float32)
    expert_gate = normal_values(key_of[6], (EXPERTS, D, FF), D ** -0.5, 0.125, ((0, 8), (2, 32)))
    expert_up = normal_values(key_of[7], (EXPERTS, D, FF), D ** -0.5, 0.125, ((0, 8), (2, 32)))
    expert_down = normal_values(key_of[8], (EXPERTS, FF, D), FF ** -0.5, 0.078125, ((0, 8), (1, 32)))
    cache_keys = draw_cache_keys(jax.random.fold_in(key_of[15], 71), 0)
    cache_values = normal_values(key_of[10], (PAGES_ALL, PAGE, HD), 2.0, 12.0, ((0, 256),))
    block_table = draw_block_table(jax.random.fold_in(key_of[15], 71), 0)
    prefix_lengths = draw_prefix_lengths(jax.random.fold_in(key_of[15], 71), 0)
    prompt_lengths = jax.vmap(lambda own: ragged(own, REQ_ROW, TOK_ROW, MOST_LEN, 2))(jax.random.split(key_of[13], GROUPS)).reshape((GROUPS, REQ_ROW)).astype(jnp.int32)
    routed_experts_keys = jax.random.split(jax.random.fold_in(key_of[14], 1), TOKENS // TOK_ROW)
    routed_experts_turns = jax.random.permutation(jax.random.fold_in(key_of[14], 3), TOKENS // TOK_ROW)
    routed_experts = jax.vmap(lambda own, number: shared_out(jax.random.fold_in(key_of[14], 2), own, number, TOK_ROW, EXPERTS, TOP, CAP, 1))(routed_experts_keys, routed_experts_turns).reshape((TOKENS, TOP))
    return {"hidden_in": hidden_in, "attn_gain": attn_gain, "qkv_weight": qkv_weight, "out_weight": out_weight, "moe_gain": moe_gain, "router_weight": router_weight, "expert_gate": expert_gate, "expert_up": expert_up, "expert_down": expert_down, "cache_keys": cache_keys, "cache_values": cache_values, "block_table": block_table, "prefix_lengths": prefix_lengths, "prompt_lengths": prompt_lengths, "routed_experts": routed_experts}


norm_epsilon = 1e-05
residual_scale = 1.4 / math.sqrt(40.0)
rotary_base = 10000.0
masked_score = -1e+30

def rotate(values, positions, head_dim):
    row_count = values.shape[0]
    head_count = values.shape[1] // head_dim
    half_dim = head_dim // 2
    frequency = rotary_base ** (-2.0 * jnp.arange(half_dim, dtype=jnp.float32) / head_dim)
    angles = positions.astype(jnp.float32)[:, None] * frequency[None, :]
    cosine = jnp.cos(angles)[:, None, :]
    sine_part = jnp.sin(angles)[:, None, :]
    shaped = values.reshape(row_count, head_count, head_dim)
    first_half = shaped[:, :, :half_dim]
    second_half = shaped[:, :, half_dim:]
    turned = jnp.concatenate([first_half * cosine - second_half * sine_part, second_half * cosine + first_half * sine_part], axis=2)
    return turned.reshape(row_count, head_count * head_dim)

def token_layout(prompt_row, prefix_row, row_count):
    run_ends = jnp.cumsum(prompt_row, dtype=jnp.int32)
    starts = run_ends - prompt_row
    offsets = jnp.arange(row_count, dtype=jnp.int32)
    request = lax.optimization_barrier(jnp.sum((offsets[:, None] >= run_ends[None, :]).astype(jnp.int32), axis=1, dtype=jnp.int32))
    member = request[:, None] == jnp.arange(prompt_row.shape[0], dtype=jnp.int32)[None, :]
    start_of = lax.optimization_barrier(jnp.sum(jnp.where(member, starts[None, :], 0), axis=1, dtype=jnp.int32))
    prefix_of = lax.optimization_barrier(jnp.sum(jnp.where(member, prefix_row[None, :], 0), axis=1, dtype=jnp.int32))
    return (request, prefix_of + offsets - start_of)

def reference(hidden_in, attn_gain, qkv_weight, out_weight, moe_gain, router_weight, expert_gate, expert_up, expert_down, cache_keys, cache_values, block_table, prefix_lengths, prompt_lengths, routed_experts):
    residual = hidden_in.astype(jnp.float32)
    scale_one = lax.rsqrt(lax.optimization_barrier(jnp.mean(residual * residual, axis=1)) + norm_epsilon)
    normed = (residual * scale_one[:, None] * attn_gain[None, :]).astype(jnp.bfloat16)
    query_raw = jnp.dot(normed, qkv_weight[:, :HD], preferred_element_type=jnp.float32)
    normed_blocks = normed.reshape(TOKENS, SHARDS, D // SHARDS).transpose(1, 0, 2)
    weight_blocks = qkv_weight[:, HD:].reshape(SHARDS, D // SHARDS, 2 * HD)

    def add_features(running, block_pair):
        value_partial_sum = lax.optimization_barrier(jnp.dot(block_pair[0], block_pair[1], preferred_element_type=jnp.float32).astype(jnp.bfloat16))
        return (running + value_partial_sum.astype(jnp.float32), None)
    key_value, ignored = lax.scan(add_features, jnp.zeros((TOKENS, 2 * HD), jnp.float32), (normed_blocks, weight_blocks))

    def layout_group(prompt_row, prefix_row):
        return token_layout(prompt_row, prefix_row, TOK_ROW)
    request, position = jax.vmap(layout_group)(prompt_lengths, prefix_lengths)
    position_flat = position.reshape(TOKENS)
    queries = (rotate(query_raw, position_flat, HEAD_DIM) * HEAD_DIM ** (-0.5)).astype(jnp.bfloat16)
    new_keys = rotate(key_value[:, :HD], position_flat, HEAD_DIM).astype(jnp.bfloat16)
    new_values = key_value[:, HD:].astype(jnp.bfloat16)
    key_share = TOK_ROW // SHARDS
    cached_block = REQ_ROW * PG_DEV * PAGE
    block_keys = cached_block + key_share
    logical = jnp.arange(MAXP, dtype=jnp.int32).reshape(PG_DEV, SHARDS)
    cached_pos = logical[:, :, None] * PAGE + jnp.arange(PAGE, dtype=jnp.int32)[None, None, :]
    cached_pos = jnp.broadcast_to(cached_pos[None], (REQ_ROW, PG_DEV, SHARDS, PAGE))
    request_ids = jnp.arange(REQ_ROW, dtype=jnp.int32)
    cached_req = jnp.broadcast_to(request_ids[:, None, None, None], (REQ_ROW, PG_DEV, SHARDS, PAGE))

    def to_blocks(table):
        return jnp.transpose(table, (2, 0, 1, 3)).reshape(SHARDS, cached_block)

    def group_attention(operands):
        query_group, key_group, value_group, request_row, position_row, table_row, prefix_row = operands
        page_keys = cache_keys[table_row].reshape(REQ_ROW, PG_DEV, SHARDS, PAGE, HD).transpose(2, 0, 1, 3, 4).reshape(SHARDS, cached_block, HD)
        page_values = cache_values[table_row].reshape(REQ_ROW, PG_DEV, SHARDS, PAGE, HD).transpose(2, 0, 1, 3, 4).reshape(SHARDS, cached_block, HD)
        live_cached = to_blocks((cached_pos < prefix_row[:, None, None, None]).astype(jnp.int32))
        all_keys = jnp.concatenate([page_keys, key_group.reshape(SHARDS, key_share, HD)], axis=1)
        all_values = jnp.concatenate([page_values, value_group.reshape(SHARDS, key_share, HD)], axis=1)
        key_live = jnp.concatenate([live_cached, jnp.ones((SHARDS, key_share), jnp.int32)], axis=1)
        key_request = jnp.concatenate([to_blocks(cached_req), request_row.reshape(SHARDS, key_share)], axis=1)
        key_position = jnp.concatenate([to_blocks(cached_pos), position_row.reshape(SHARDS, key_share)], axis=1)
        allowed = (request_row[:, None, None] == key_request[None]) & (key_live[None] > 0) & (key_position[None] <= position_row[:, None, None])
        key_heads = all_keys.reshape(SHARDS, block_keys, HEADS, HEAD_DIM).transpose(2, 0, 1, 3)
        value_heads = all_values.reshape(SHARDS, block_keys, HEADS, HEAD_DIM).transpose(2, 0, 1, 3)
        query_heads = query_group.reshape(TOK_ROW, HEADS, HEAD_DIM).transpose(1, 0, 2)

        def one_head(head_operands):
            single_query, single_key, single_value = head_operands
            score_matrix = jnp.einsum('yj,fpj->yfp', single_query.astype(jnp.float32), single_key.astype(jnp.float32))
            score_matrix = jnp.where(allowed, score_matrix, masked_score)
            block_max = lax.optimization_barrier(jnp.max(score_matrix, axis=2))
            largest = lax.optimization_barrier(jnp.max(block_max, axis=1))
            exponent = jnp.where(allowed, jnp.exp(score_matrix - block_max[:, :, None]), 0.0)
            factor = jnp.exp(block_max - largest[:, None])
            total_weight = lax.optimization_barrier(jnp.sum(lax.optimization_barrier(jnp.sum(exponent, axis=2)) * factor, axis=1))
            weight_tensors = exponent.astype(jnp.bfloat16)
            value_partial_sum = jnp.einsum('exz,xzn->exn', weight_tensors.astype(jnp.float32), single_value.astype(jnp.float32))
            summed = lax.optimization_barrier(jnp.sum(value_partial_sum * factor[:, :, None], axis=1))
            return (summed / total_weight[:, None]).astype(jnp.bfloat16)
        attended_heads = lax.map(one_head, (query_heads, key_heads, value_heads))
        return attended_heads.transpose(1, 0, 2).reshape(TOK_ROW, HD)
    attended = lax.map(group_attention, (queries.reshape(GROUPS, TOK_ROW, HD), new_keys.reshape(GROUPS, TOK_ROW, HD), new_values.reshape(GROUPS, TOK_ROW, HD), request, position, block_table, prefix_lengths))
    attended = attended.reshape(TOKENS, HD)
    attn_out = jnp.dot(attended, out_weight, preferred_element_type=jnp.float32).astype(jnp.bfloat16)
    middle = (residual + residual_scale * attn_out.astype(jnp.float32)).astype(jnp.bfloat16)
    middle_wide = middle.astype(jnp.float32)
    scale_two = lax.rsqrt(lax.optimization_barrier(jnp.mean(middle_wide * middle_wide, axis=1)) + norm_epsilon)
    moe_normed_f = middle_wide * scale_two[:, None] * moe_gain[None, :]
    moe_normed = moe_normed_f.astype(jnp.bfloat16)
    logits = jnp.dot(moe_normed_f, router_weight, precision=lax.Precision.HIGHEST)
    onehot_three = routed_experts[:, :, None] == jnp.arange(EXPERTS, dtype=jnp.int32)[None, None, :]
    selected_logits = lax.optimization_barrier(jnp.sum(jnp.where(onehot_three, logits[:, None, :], 0.0), axis=2))
    first_gate = jax.nn.sigmoid(selected_logits[:, 0] - selected_logits[:, 1])
    gate_pair = jnp.stack([first_gate, 1.0 - first_gate], axis=1)
    grouped = onehot_three.astype(jnp.int32).reshape(GROUPS, TOK_ROW * TOP, EXPERTS)
    earlier = jnp.cumsum(grouped, axis=1, dtype=jnp.int32) - grouped
    slot_index = lax.optimization_barrier(jnp.sum(earlier * grouped, axis=2, dtype=jnp.int32))
    chosen = routed_experts.reshape(GROUPS, TOK_ROW * TOP)
    target = chosen * CAP + slot_index
    token_local = jnp.arange(TOK_ROW * TOP, dtype=jnp.int32) // TOP

    def fill_group(target_row):
        source = jnp.zeros((EXPERTS * CAP,), jnp.int32).at[target_row].set(token_local)
        filled = jnp.zeros((EXPERTS * CAP,), jnp.int32).at[target_row].set(1)
        return (source, filled)
    source, filled = jax.vmap(fill_group)(target)
    source_global = source + jnp.arange(GROUPS, dtype=jnp.int32)[:, None] * TOK_ROW
    gathered = jnp.where(filled[:, :, None] > 0, moe_normed[source_global], jnp.zeros((), jnp.bfloat16))
    expert_inputs = gathered.reshape(GROUPS, EXPERTS, CAP, D).transpose(1, 0, 2, 3).reshape(EXPERTS, GROUPS * CAP, D)

    def one_expert(operands):
        inputs_one, gate_one, up_one, down_one = operands
        gate_act = jnp.dot(inputs_one, gate_one, preferred_element_type=jnp.float32)
        up_act = jnp.dot(inputs_one, up_one, preferred_element_type=jnp.float32)
        hidden = (jax.nn.silu(gate_act) * up_act).astype(jnp.bfloat16)
        hidden_blocks = hidden.reshape(GROUPS * CAP, SHARDS, FF // SHARDS).transpose(1, 0, 2)
        down_blocks = down_one.reshape(SHARDS, FF // SHARDS, D)

        def add_block(running, block_pair):
            value_partial_sum = lax.optimization_barrier(jnp.dot(block_pair[0], block_pair[1], preferred_element_type=jnp.float32).astype(jnp.bfloat16))
            return (running + value_partial_sum.astype(jnp.float32), None)
        summed, unused = lax.scan(add_block, jnp.zeros((GROUPS * CAP, D), jnp.float32), (hidden_blocks, down_blocks))
        return summed.astype(jnp.bfloat16)
    expert_result = lax.map(one_expert, (expert_inputs, expert_gate, expert_up, expert_down))
    result_row = jnp.arange(GROUPS, dtype=jnp.int32)[:, None] * CAP + slot_index
    picked = expert_result[chosen, result_row].reshape(TOKENS, TOP, D).astype(jnp.float32)
    moe_out = lax.optimization_barrier(jnp.sum(picked * gate_pair[:, :, None], axis=1)).astype(jnp.bfloat16)
    layer_out = (middle_wide + residual_scale * moe_out.astype(jnp.float32)).astype(jnp.bfloat16)
    return (attn_out, moe_out, layer_out)
```

```python
import math

import jax
import jax.numpy as jnp
from jax import lax
from jax.sharding import PartitionSpec as P

D = 2304
HEAD_DIM = 64
TOP = 2


norm_epsilon = 1e-05
residual_scale = 1.4 / math.sqrt(40.0)
rotary_base = 10000.0
masked_score = -1e30


def merged(value, axis, join):
    pieces = jax.tree.map(lambda part: lax.all_gather(part, axis), value)
    head = jax.tree.map(lambda part: part[0], pieces)
    tail = jax.tree.map(lambda part: part[1:], pieces)
    running, _ = lax.scan(lambda running, slab: (join(running, slab), None), head, tail)
    return running


def rotate(values, positions, head_dim):
    row_count = values.shape[0]
    head_count = values.shape[1] // head_dim
    half_dim = head_dim // 2
    frequency = rotary_base ** (-2.0 * jnp.arange(half_dim, dtype=jnp.float32) / head_dim)
    angles = positions.astype(jnp.float32)[:, None] * frequency[None, :]
    cosine = jnp.cos(angles)[:, None, :]
    sine_part = jnp.sin(angles)[:, None, :]
    shaped = values.reshape(row_count, head_count, head_dim)
    first_half = shaped[:, :, :half_dim]
    second_half = shaped[:, :, half_dim:]
    turned = jnp.concatenate(
        [
            first_half * cosine - second_half * sine_part,
            second_half * cosine + first_half * sine_part,
        ],
        axis=2,
    )
    return turned.reshape(row_count, head_count * head_dim)


def token_layout(prompt_row, prefix_row, row_count):
    run_ends = jnp.cumsum(prompt_row, dtype=jnp.int32)
    starts = run_ends - prompt_row
    offsets = jnp.arange(row_count, dtype=jnp.int32)
    request = jnp.sum(
        (offsets[:, None] >= run_ends[None, :]).astype(jnp.int32), axis=1, dtype=jnp.int32
    )
    member = request[:, None] == jnp.arange(prompt_row.shape[0], dtype=jnp.int32)[None, :]
    start_of = jnp.sum(jnp.where(member, starts[None, :], 0), axis=1, dtype=jnp.int32)
    prefix_of = jnp.sum(jnp.where(member, prefix_row[None, :], 0), axis=1, dtype=jnp.int32)
    return (request, prefix_of + offsets - start_of)


def rescale(summed, factor):
    group_count, row_count, feature_width = summed.shape
    group_size = factor.shape[1]
    shaped = summed.reshape(group_count, row_count, group_size, feature_width // group_size)
    shaped = shaped * jnp.transpose(factor, (0, 2, 1))[:, :, :, None]
    return shaped.reshape(group_count, row_count, feature_width)


def divide_rows(summed, total_weight):
    group_count, row_count, feature_width = summed.shape
    group_size = total_weight.shape[1]
    shaped = summed.reshape(group_count, row_count, group_size, feature_width // group_size)
    shaped = shaped / jnp.transpose(total_weight, (0, 2, 1))[:, :, :, None]
    return shaped.reshape(group_count, row_count, feature_width)


def combine_parts(earlier_part, later_part):
    largest = jnp.maximum(earlier_part[0], later_part[0])
    factor_one = jnp.exp(earlier_part[0] - largest)
    factor_two = jnp.exp(later_part[0] - largest)
    total_weight = earlier_part[1] * factor_one + later_part[1] * factor_two
    summed = rescale(earlier_part[2], factor_one) + rescale(later_part[2], factor_two)
    return (largest, total_weight, summed)


def on_device(
    hidden_in,
    attn_gain,
    qkv_weight,
    out_weight,
    moe_gain,
    router_weight,
    expert_gate,
    expert_up,
    expert_down,
    cache_keys,
    cache_values,
    block_table,
    prefix_lengths,
    prompt_lengths,
    routed_experts,
):
    col_count = lax.axis_size("col")
    row_devices = lax.axis_size("row")
    col_index = lax.axis_index("col")
    row_index = lax.axis_index("row")
    tok_rows = hidden_in.shape[0]
    feature_width = hidden_in.shape[1]
    head_total = out_weight.shape[0]
    head_count = head_total // HEAD_DIM
    key_share = tok_rows // col_count
    request, position = token_layout(prompt_lengths[0], prefix_lengths[0], tok_rows)
    own_start = col_index * key_share
    key_position = lax.dynamic_slice_in_dim(position, own_start, key_share)
    key_request = lax.dynamic_slice_in_dim(request, own_start, key_share)
    residual = hidden_in.astype(jnp.float32)
    squares = jnp.sum(lax.all_gather(jnp.sum(residual * residual, axis=1), "col"), axis=0)
    scale_one = lax.rsqrt(squares / D + norm_epsilon)
    normed = (residual * scale_one[:, None] * attn_gain[None, :]).astype(jnp.bfloat16)
    query_part = jnp.dot(normed, qkv_weight[:, :head_total], preferred_element_type=jnp.float32)
    query_sum = lax.psum(query_part, "col")
    queries = (rotate(query_sum, position, HEAD_DIM) * HEAD_DIM ** (-0.5)).astype(jnp.bfloat16)
    kv_part = jnp.dot(
        normed, qkv_weight[:, head_total:], preferred_element_type=jnp.float32
    ).astype(jnp.bfloat16)
    kv_width = kv_part.shape[1]
    key_value = (
        lax.psum_scatter(
            kv_part.reshape(col_count * 8, key_share * kv_width // 8),
            "col",
            scatter_dimension=0,
            tiled=True,
        )
        .reshape(key_share, kv_width)
        .astype(jnp.float32)
    )
    new_keys = rotate(key_value[:, :head_total], key_position, HEAD_DIM).astype(jnp.bfloat16)
    new_values = key_value[:, head_total:].astype(jnp.bfloat16)
    pool_size = cache_keys.shape[0]
    page_size = cache_keys.shape[1]
    req_count = block_table.shape[1]
    pages_each = block_table.shape[2] // col_count
    page_table = block_table[0].reshape(req_count, pages_each, col_count)
    own_pages = lax.dynamic_slice_in_dim(page_table, col_index, 1, 2).reshape(
        req_count * pages_each
    )
    pool_offset_begin = (row_index * col_count + col_index) * pool_size
    slot_ids = jnp.arange(pool_size, dtype=jnp.int32)
    entry_ids = jnp.arange(req_count * pages_each, dtype=jnp.int32)
    slot_match = (own_pages - pool_offset_begin)[None, :] == slot_ids[:, None]
    entry_request = entry_ids // pages_each
    entry_page = entry_ids % pages_each * col_count + col_index
    slot_request = jnp.sum(
        jnp.where(slot_match, entry_request[None, :], 0), axis=1, dtype=jnp.int32
    )
    slot_page = jnp.sum(jnp.where(slot_match, entry_page[None, :], 0), axis=1, dtype=jnp.int32)
    prefix_row = prefix_lengths[0]
    slot_prefix = jnp.sum(
        jnp.where(
            slot_request[:, None] == jnp.arange(req_count, dtype=jnp.int32)[None, :],
            prefix_row[None, :],
            0,
        ),
        axis=1,
        dtype=jnp.int32,
    )
    cache_position = (
        slot_page[:, None] * page_size + jnp.arange(page_size, dtype=jnp.int32)[None, :]
    )
    cache_live = (
        (cache_position < slot_prefix[:, None]).astype(jnp.int32).reshape(pool_size * page_size)
    )
    cache_request = jnp.broadcast_to(slot_request[:, None], (pool_size, page_size)).reshape(
        pool_size * page_size
    )
    cache_mask = (request[:, None] == cache_request[None, :]) & (cache_live[None, :] > 0)
    fresh_mask = (request[:, None] == key_request[None, :]) & (
        key_position[None, :] <= position[:, None]
    )
    query_heads = queries.reshape(tok_rows, head_count, HEAD_DIM)
    key_heads = jnp.concatenate(
        [cache_keys.reshape(pool_size * page_size, head_total), new_keys], axis=0
    ).reshape(pool_size * page_size + key_share, head_count, HEAD_DIM)
    value_heads = jnp.concatenate(
        [cache_values.reshape(pool_size * page_size, head_total), new_values], axis=0
    ).reshape(pool_size * page_size + key_share, head_count, HEAD_DIM)
    key_mask = jnp.concatenate([cache_mask, fresh_mask], axis=1)
    score_matrix = jnp.einsum(
        "thd,khd->htk", query_heads, key_heads, preferred_element_type=jnp.float32
    )
    score_matrix = jnp.where(key_mask[None], score_matrix, masked_score)
    local_max = jnp.max(score_matrix, axis=2)
    weights = jnp.where(key_mask[None], jnp.exp(score_matrix - local_max[:, :, None]), 0.0)
    local_total = jnp.sum(weights, axis=2)
    local_sum = jnp.einsum(
        "htk,khd->thd",
        weights.astype(jnp.bfloat16),
        value_heads,
        preferred_element_type=jnp.float32,
    )
    largest = jnp.max(lax.all_gather(local_max, "col"), axis=0)
    factor = jnp.exp(local_max - largest)
    scaled_sum = local_sum * jnp.transpose(factor)[:, :, None]
    scaled_total = jnp.transpose(local_total * factor)
    joined = lax.psum(
        jnp.concatenate([scaled_sum.reshape(tok_rows, head_total), scaled_total], axis=1), "col"
    )
    summed = joined[:, :head_total].reshape(tok_rows, head_count, HEAD_DIM)
    total_weight = joined[:, head_total:]
    attended = (summed / total_weight[:, :, None]).reshape(tok_rows, head_total).astype(
        jnp.bfloat16
    )
    projected = jnp.dot(attended, out_weight, preferred_element_type=jnp.float32)
    attn_out = projected.astype(jnp.bfloat16)
    middle = (residual + residual_scale * attn_out.astype(jnp.float32)).astype(jnp.bfloat16)
    middle_wide = middle.astype(jnp.float32)
    router_part = jnp.dot(
        middle_wide * moe_gain[None, :], router_weight, precision=lax.Precision.HIGHEST
    )
    stats = jnp.sum(
        lax.all_gather(
            jnp.concatenate(
                [jnp.sum(middle_wide * middle_wide, axis=1, keepdims=True), router_part], axis=1
            ),
            "col",
        ),
        axis=0,
    )
    scale_two = lax.rsqrt(stats[:, 0] / D + norm_epsilon)
    moe_normed_f = middle_wide * scale_two[:, None] * moe_gain[None, :]
    logits = stats[:, 1:] * scale_two[:, None]
    moe_normed = moe_normed_f.astype(jnp.bfloat16)
    expert_local = expert_gate.shape[0]
    expert_total = expert_local * row_devices
    capacity = 2 * TOP * tok_rows // expert_total
    onehot_three = (
        routed_experts[:, :, None] == jnp.arange(expert_total, dtype=jnp.int32)[None, None, :]
    )
    selected_logits = jnp.sum(jnp.where(onehot_three, logits[:, None, :], 0.0), axis=2)
    first_gate = jax.nn.sigmoid(selected_logits[:, 0] - selected_logits[:, 1])
    gate_pair = jnp.stack([first_gate, 1.0 - first_gate], axis=1)
    onehot = onehot_three.astype(jnp.int32).reshape(tok_rows * TOP, expert_total)
    earlier = jnp.cumsum(onehot, axis=0, dtype=jnp.int32) - onehot
    slot_index = jnp.sum(earlier * onehot, axis=1, dtype=jnp.int32)
    target = routed_experts.reshape(tok_rows * TOP) * capacity + slot_index
    token_local = jnp.arange(tok_rows * TOP, dtype=jnp.int32) // TOP
    source = jnp.zeros((expert_total * capacity,), jnp.int32).at[target].set(token_local)
    filled = jnp.zeros((expert_total * capacity,), jnp.int32).at[target].set(1)
    outgoing = jnp.where(
        filled[:, None] > 0, moe_normed[source], jnp.zeros((), jnp.bfloat16)
    ).reshape(expert_total, capacity, feature_width)
    arrived = lax.all_to_all(outgoing, "row", split_axis=0, concat_axis=0, tiled=True)
    expert_rows = (
        arrived.reshape(row_devices, expert_local, capacity, feature_width)
        .transpose(1, 0, 2, 3)
        .reshape(expert_local, row_devices * capacity, feature_width)
    )
    feature_piece = lax.all_gather(expert_rows, "col", axis=2, tiled=True)
    gate_next = jnp.einsum(
        "erd,edf->erf", feature_piece, expert_gate, preferred_element_type=jnp.float32
    )
    up_next = jnp.einsum(
        "erd,edf->erf", feature_piece, expert_up, preferred_element_type=jnp.float32
    )
    hidden = (jax.nn.silu(gate_next) * up_next).astype(jnp.bfloat16)
    received_rows = hidden.shape[1]
    value_partial_sum = jnp.einsum(
        "efo,erf->oer", expert_down, hidden, preferred_element_type=jnp.float32
    )
    expert_out = lax.psum_scatter(
        value_partial_sum.reshape(
            lax.axis_size("col") * feature_width, expert_local * received_rows
        ).astype(jnp.bfloat16),
        "col",
        scatter_dimension=0,
        tiled=True,
    )
    returned = lax.all_to_all(
        expert_out.reshape(feature_width, expert_local, received_rows),
        "row",
        split_axis=2,
        concat_axis=1,
        tiled=True,
    )
    flat_back = returned.reshape(feature_width, expert_total * capacity)
    picked = (
        jnp.take(flat_back, target, axis=1)
        .astype(jnp.float32)
        .reshape(feature_width, tok_rows, TOP)
    )
    moe_columns = jnp.sum(picked * gate_pair[None, :, :], axis=2).astype(jnp.bfloat16)
    moe_out = moe_columns.T
    layer_out = (middle_wide + residual_scale * moe_out.astype(jnp.float32)).astype(jnp.bfloat16)
    return (attn_out, moe_out, layer_out)


def solution(mesh):
    in_specs = (
        P("row", "col"),
        P("col"),
        P("col", None),
        P(None, "col"),
        P("col"),
        P("col", None),
        P("row", None, "col"),
        P("row", None, "col"),
        P("row", "col", None),
        P(("row", "col"), None, None),
        P(("row", "col"), None, None),
        P("row", None, None),
        P("row", None),
        P("row", None),
        P("row", None),
    )
    out_specs = (P("row", "col"), P("row", "col"), P("row", "col"))
    return jax.shard_map(
        on_device, mesh=mesh, in_specs=in_specs, out_specs=out_specs, check_vma=False
    )
```

```python
import math

import jax
import jax.numpy as jnp
from jax import lax
from jax.sharding import PartitionSpec as P

D = 2304
HEAD_DIM = 64
TOP = 2


norm_epsilon = 1e-05
residual_scale = 1.4 / math.sqrt(40.0)
rotary_base = 10000.0
masked_score = -1e30


def merged(value, axis, join):
    pieces = jax.tree.map(lambda part: lax.all_gather(part, axis), value)
    head = jax.tree.map(lambda part: part[0], pieces)
    tail = jax.tree.map(lambda part: part[1:], pieces)
    running, _ = lax.scan(lambda running, slab: (join(running, slab), None), head, tail)
    return running


def partner_swap(value, axis, bit, count):
    pairs = [(device, device ^ (1 << bit)) for device in range(count)]
    return lax.ppermute(value, axis, pairs)


def tree_scatter(chunks, axis, bits, join):
    count = chunks.shape[0]
    depth = count.bit_length() - 1
    me = lax.axis_index(axis)
    present = list(range(depth - 1, -1, -1))
    buffer = chunks.reshape((2,) * depth + chunks.shape[1:])
    for bit in bits:
        place = present.index(bit)
        mine = (me >> bit) & 1
        low = lax.index_in_dim(buffer, 0, place, keepdims=False)
        high = lax.index_in_dim(buffer, 1, place, keepdims=False)
        keep = jnp.where(mine > 0, high, low)
        send = jnp.where(mine > 0, low, high)
        buffer = join(keep, partner_swap(send, axis, bit, count))
        present.pop(place)
    return buffer


def tree_gather(piece, axis, bits, count):
    me = lax.axis_index(axis)
    present = []
    buffer = piece
    for bit in bits:
        mine = (me >> bit) & 1
        other = partner_swap(buffer, axis, bit, count)
        low = jnp.where(mine > 0, other, buffer)
        high = jnp.where(mine > 0, buffer, other)
        buffer = jnp.stack([low, high], axis=0)
        present.insert(0, bit)
    order = sorted(range(len(present)), key=lambda place: -present[place])
    buffer = jnp.transpose(buffer, order + list(range(len(present), buffer.ndim)))
    return buffer.reshape((count,) + piece.shape)


def add_wide(keep, other):
    return keep.astype(jnp.float32) + other.astype(jnp.float32)


def join_softmax(keep, other):
    width = keep.shape[-1] - 2
    largest = jnp.maximum(keep[..., width], other[..., width])
    factor_keep = jnp.exp(keep[..., width] - largest)
    factor_other = jnp.exp(other[..., width] - largest)
    summed = keep[..., :width] * factor_keep[..., None] + other[..., :width] * factor_other[..., None]
    total = keep[..., width + 1] * factor_keep + other[..., width + 1] * factor_other
    return jnp.concatenate([summed, largest[..., None], total[..., None]], axis=-1)


def rotate(values, positions, head_dim):
    row_count = values.shape[0]
    head_count = values.shape[1] // head_dim
    half_dim = head_dim // 2
    frequency = rotary_base ** (-2.0 * jnp.arange(half_dim, dtype=jnp.float32) / head_dim)
    angles = positions.astype(jnp.float32)[:, None] * frequency[None, :]
    cosine = jnp.cos(angles)[:, None, :]
    sine_part = jnp.sin(angles)[:, None, :]
    shaped = values.reshape(row_count, head_count, head_dim)
    first_half = shaped[:, :, :half_dim]
    second_half = shaped[:, :, half_dim:]
    turned = jnp.concatenate(
        [
            first_half * cosine - second_half * sine_part,
            second_half * cosine + first_half * sine_part,
        ],
        axis=2,
    )
    return turned.reshape(row_count, head_count * head_dim)


def token_layout(prompt_row, prefix_row, row_count):
    run_ends = jnp.cumsum(prompt_row, dtype=jnp.int32)
    starts = run_ends - prompt_row
    offsets = jnp.arange(row_count, dtype=jnp.int32)
    request = jnp.sum(
        (offsets[:, None] >= run_ends[None, :]).astype(jnp.int32), axis=1, dtype=jnp.int32
    )
    member = request[:, None] == jnp.arange(prompt_row.shape[0], dtype=jnp.int32)[None, :]
    start_of = jnp.sum(jnp.where(member, starts[None, :], 0), axis=1, dtype=jnp.int32)
    prefix_of = jnp.sum(jnp.where(member, prefix_row[None, :], 0), axis=1, dtype=jnp.int32)
    return (request, prefix_of + offsets - start_of)


def rescale(summed, factor):
    group_count, row_count, feature_width = summed.shape
    group_size = factor.shape[1]
    shaped = summed.reshape(group_count, row_count, group_size, feature_width // group_size)
    shaped = shaped * jnp.transpose(factor, (0, 2, 1))[:, :, :, None]
    return shaped.reshape(group_count, row_count, feature_width)


def divide_rows(summed, total_weight):
    group_count, row_count, feature_width = summed.shape
    group_size = total_weight.shape[1]
    shaped = summed.reshape(group_count, row_count, group_size, feature_width // group_size)
    shaped = shaped / jnp.transpose(total_weight, (0, 2, 1))[:, :, :, None]
    return shaped.reshape(group_count, row_count, feature_width)


def combine_parts(earlier_part, later_part):
    largest = jnp.maximum(earlier_part[0], later_part[0])
    factor_one = jnp.exp(earlier_part[0] - largest)
    factor_two = jnp.exp(later_part[0] - largest)
    total_weight = earlier_part[1] * factor_one + later_part[1] * factor_two
    summed = rescale(earlier_part[2], factor_one) + rescale(later_part[2], factor_two)
    return (largest, total_weight, summed)


def on_device(
    hidden_in,
    attn_gain,
    qkv_weight,
    out_weight,
    moe_gain,
    router_weight,
    expert_gate,
    expert_up,
    expert_down,
    cache_keys,
    cache_values,
    block_table,
    prefix_lengths,
    prompt_lengths,
    routed_experts,
):
    col_count = lax.axis_size("col")
    row_devices = lax.axis_size("row")
    col_index = lax.axis_index("col")
    row_index = lax.axis_index("row")
    tok_rows = hidden_in.shape[0]
    feature_width = hidden_in.shape[1]
    head_total = out_weight.shape[0]
    head_count = head_total // HEAD_DIM
    key_share = tok_rows // col_count
    request, position = token_layout(prompt_lengths[0], prefix_lengths[0], tok_rows)
    own_start = col_index * key_share
    key_position = lax.dynamic_slice_in_dim(position, own_start, key_share)
    key_request = lax.dynamic_slice_in_dim(request, own_start, key_share)
    residual = hidden_in.astype(jnp.float32)
    squares = jnp.sum(lax.all_gather(jnp.sum(residual * residual, axis=1), "col"), axis=0)
    scale_one = lax.rsqrt(squares / D + norm_epsilon)
    normed = (residual * scale_one[:, None] * attn_gain[None, :]).astype(jnp.bfloat16)
    scatter_bits = [0] + list(range(1, col_count.bit_length() - 1))
    gather_bits = scatter_bits[::-1]
    query_part = jnp.dot(normed, qkv_weight[:, :head_total], preferred_element_type=jnp.float32)
    kv_part = jnp.dot(
        normed, qkv_weight[:, head_total:], preferred_element_type=jnp.float32
    ).astype(jnp.bfloat16)
    both_part = jnp.concatenate([query_part, kv_part.astype(jnp.float32)], axis=1)
    both_sum = tree_scatter(
        both_part.reshape(col_count, key_share, both_part.shape[1]), "col", scatter_bits, add_wide
    )
    own_queries = (
        rotate(both_sum[:, :head_total], key_position, HEAD_DIM) * HEAD_DIM ** (-0.5)
    ).astype(jnp.bfloat16)
    queries = tree_gather(own_queries, "col", gather_bits, col_count).reshape(
        tok_rows, head_total
    )
    key_value = both_sum[:, head_total:]
    new_keys = rotate(key_value[:, :head_total], key_position, HEAD_DIM).astype(jnp.bfloat16)
    new_values = key_value[:, head_total:].astype(jnp.bfloat16)
    pool_size = cache_keys.shape[0]
    page_size = cache_keys.shape[1]
    req_count = block_table.shape[1]
    pages_each = block_table.shape[2] // col_count
    page_table = block_table[0].reshape(req_count, pages_each, col_count)
    own_pages = lax.dynamic_slice_in_dim(page_table, col_index, 1, 2).reshape(
        req_count * pages_each
    )
    pool_offset_begin = (row_index * col_count + col_index) * pool_size
    slot_ids = jnp.arange(pool_size, dtype=jnp.int32)
    entry_ids = jnp.arange(req_count * pages_each, dtype=jnp.int32)
    slot_match = (own_pages - pool_offset_begin)[None, :] == slot_ids[:, None]
    entry_request = entry_ids // pages_each
    entry_page = entry_ids % pages_each * col_count + col_index
    slot_request = jnp.sum(
        jnp.where(slot_match, entry_request[None, :], 0), axis=1, dtype=jnp.int32
    )
    slot_page = jnp.sum(jnp.where(slot_match, entry_page[None, :], 0), axis=1, dtype=jnp.int32)
    prefix_row = prefix_lengths[0]
    slot_prefix = jnp.sum(
        jnp.where(
            slot_request[:, None] == jnp.arange(req_count, dtype=jnp.int32)[None, :],
            prefix_row[None, :],
            0,
        ),
        axis=1,
        dtype=jnp.int32,
    )
    cache_position = (
        slot_page[:, None] * page_size + jnp.arange(page_size, dtype=jnp.int32)[None, :]
    )
    cache_live = (
        (cache_position < slot_prefix[:, None]).astype(jnp.int32).reshape(pool_size * page_size)
    )
    cache_request = jnp.broadcast_to(slot_request[:, None], (pool_size, page_size)).reshape(
        pool_size * page_size
    )
    cache_mask = (request[:, None] == cache_request[None, :]) & (cache_live[None, :] > 0)
    fresh_mask = (request[:, None] == key_request[None, :]) & (
        key_position[None, :] <= position[:, None]
    )
    query_heads = queries.reshape(tok_rows, head_count, HEAD_DIM)
    key_heads = jnp.concatenate(
        [cache_keys.reshape(pool_size * page_size, head_total), new_keys], axis=0
    ).reshape(pool_size * page_size + key_share, head_count, HEAD_DIM)
    value_heads = jnp.concatenate(
        [cache_values.reshape(pool_size * page_size, head_total), new_values], axis=0
    ).reshape(pool_size * page_size + key_share, head_count, HEAD_DIM)
    key_mask = jnp.concatenate([cache_mask, fresh_mask], axis=1)
    score_matrix = jnp.einsum(
        "thd,khd->htk", query_heads, key_heads, preferred_element_type=jnp.float32
    )
    score_matrix = jnp.where(key_mask[None], score_matrix, masked_score)
    local_max = jnp.max(score_matrix, axis=2)
    weights = jnp.where(key_mask[None], jnp.exp(score_matrix - local_max[:, :, None]), 0.0)
    local_total = jnp.sum(weights, axis=2)
    local_sum = jnp.einsum(
        "htk,khd->thd",
        weights.astype(jnp.bfloat16),
        value_heads,
        preferred_element_type=jnp.float32,
    )
    packed = jnp.concatenate(
        [
            local_sum,
            jnp.transpose(local_max)[:, :, None],
            jnp.transpose(local_total)[:, :, None],
        ],
        axis=2,
    )
    merged_rows = tree_scatter(
        packed.reshape((col_count, key_share) + packed.shape[1:]), "col", scatter_bits, join_softmax
    )
    own_attended = (
        merged_rows[..., :HEAD_DIM] / merged_rows[..., HEAD_DIM + 1][..., None]
    ).reshape(key_share, head_total).astype(jnp.bfloat16)
    attended = tree_gather(own_attended, "col", gather_bits, col_count).reshape(
        tok_rows, head_total
    )
    projected = jnp.dot(attended, out_weight, preferred_element_type=jnp.float32)
    attn_out = projected.astype(jnp.bfloat16)
    middle = (residual + residual_scale * attn_out.astype(jnp.float32)).astype(jnp.bfloat16)
    middle_wide = middle.astype(jnp.float32)
    router_part = jnp.dot(
        middle_wide * moe_gain[None, :], router_weight, precision=lax.Precision.HIGHEST
    )
    stats = jnp.sum(
        lax.all_gather(
            jnp.concatenate(
                [jnp.sum(middle_wide * middle_wide, axis=1, keepdims=True), router_part], axis=1
            ),
            "col",
        ),
        axis=0,
    )
    scale_two = lax.rsqrt(stats[:, 0] / D + norm_epsilon)
    moe_normed_f = middle_wide * scale_two[:, None] * moe_gain[None, :]
    logits = stats[:, 1:] * scale_two[:, None]
    moe_normed = moe_normed_f.astype(jnp.bfloat16)
    expert_local = expert_gate.shape[0]
    expert_total = expert_local * row_devices
    capacity = 2 * TOP * tok_rows // expert_total
    onehot_three = (
        routed_experts[:, :, None] == jnp.arange(expert_total, dtype=jnp.int32)[None, None, :]
    )
    selected_logits = jnp.sum(jnp.where(onehot_three, logits[:, None, :], 0.0), axis=2)
    first_gate = jax.nn.sigmoid(selected_logits[:, 0] - selected_logits[:, 1])
    gate_pair = jnp.stack([first_gate, 1.0 - first_gate], axis=1)
    onehot = onehot_three.astype(jnp.int32).reshape(tok_rows * TOP, expert_total)
    earlier = jnp.cumsum(onehot, axis=0, dtype=jnp.int32) - onehot
    slot_index = jnp.sum(earlier * onehot, axis=1, dtype=jnp.int32)
    target = routed_experts.reshape(tok_rows * TOP) * capacity + slot_index
    token_local = jnp.arange(tok_rows * TOP, dtype=jnp.int32) // TOP
    source = jnp.zeros((expert_total * capacity,), jnp.int32).at[target].set(token_local)
    filled = jnp.zeros((expert_total * capacity,), jnp.int32).at[target].set(1)
    outgoing = jnp.where(
        filled[:, None] > 0, moe_normed[source], jnp.zeros((), jnp.bfloat16)
    ).reshape(expert_total, capacity, feature_width)
    arrived = lax.all_to_all(outgoing, "row", split_axis=0, concat_axis=0, tiled=True)
    expert_rows = (
        arrived.reshape(row_devices, expert_local, capacity, feature_width)
        .transpose(1, 0, 2, 3)
        .reshape(expert_local, row_devices * capacity, feature_width)
    )
    feature_piece = lax.all_gather(expert_rows, "col", axis=2, tiled=True)
    gate_next = jnp.einsum(
        "erd,edf->erf", feature_piece, expert_gate, preferred_element_type=jnp.float32
    )
    up_next = jnp.einsum(
        "erd,edf->erf", feature_piece, expert_up, preferred_element_type=jnp.float32
    )
    hidden = (jax.nn.silu(gate_next) * up_next).astype(jnp.bfloat16)
    received_rows = hidden.shape[1]
    value_partial_sum = jnp.einsum(
        "efo,erf->oer", expert_down, hidden, preferred_element_type=jnp.float32
    )
    expert_out = lax.psum_scatter(
        value_partial_sum.reshape(
            lax.axis_size("col") * feature_width, expert_local * received_rows
        ).astype(jnp.bfloat16),
        "col",
        scatter_dimension=0,
        tiled=True,
    )
    returned = lax.all_to_all(
        expert_out.reshape(feature_width, expert_local, received_rows),
        "row",
        split_axis=2,
        concat_axis=1,
        tiled=True,
    )
    flat_back = returned.reshape(feature_width, expert_total * capacity)
    picked = (
        jnp.take(flat_back, target, axis=1)
        .astype(jnp.float32)
        .reshape(feature_width, tok_rows, TOP)
    )
    moe_columns = jnp.sum(picked * gate_pair[None, :, :], axis=2).astype(jnp.bfloat16)
    moe_out = moe_columns.T
    layer_out = (middle_wide + residual_scale * moe_out.astype(jnp.float32)).astype(jnp.bfloat16)
    return (attn_out, moe_out, layer_out)


def solution(mesh):
    in_specs = (
        P("row", "col"),
        P("col"),
        P("col", None),
        P(None, "col"),
        P("col"),
        P("col", None),
        P("row", None, "col"),
        P("row", None, "col"),
        P("row", "col", None),
        P(("row", "col"), None, None),
        P(("row", "col"), None, None),
        P("row", None, None),
        P("row", None),
        P("row", None),
        P("row", None),
    )
    out_specs = (P("row", "col"), P("row", "col"), P("row", "col"))
    return jax.shard_map(
        on_device, mesh=mesh, in_specs=in_specs, out_specs=out_specs, check_vma=False
    )
```

```python
import math

import jax
import jax.numpy as jnp
from jax import lax
from jax.sharding import PartitionSpec as P

D = 2304
HEAD_DIM = 64
TOP = 2


norm_epsilon = 1e-05
residual_scale = 1.4 / math.sqrt(40.0)
rotary_base = 10000.0
masked_score = -1e30


def merged(value, axis, join):
    pieces = jax.tree.map(lambda part: lax.all_gather(part, axis), value)
    head = jax.tree.map(lambda part: part[0], pieces)
    tail = jax.tree.map(lambda part: part[1:], pieces)
    running, _ = lax.scan(lambda running, slab: (join(running, slab), None), head, tail)
    return running


def partner_swap(value, axis, bit, count):
    pairs = [(device, device ^ (1 << bit)) for device in range(count)]
    return lax.ppermute(value, axis, pairs)


def tree_scatter(chunks, axis, bits, join):
    count = chunks.shape[0]
    depth = count.bit_length() - 1
    me = lax.axis_index(axis)
    present = list(range(depth - 1, -1, -1))
    buffer = chunks.reshape((2,) * depth + chunks.shape[1:])
    for bit in bits:
        place = present.index(bit)
        mine = (me >> bit) & 1
        low = lax.index_in_dim(buffer, 0, place, keepdims=False)
        high = lax.index_in_dim(buffer, 1, place, keepdims=False)
        keep = jnp.where(mine > 0, high, low)
        send = jnp.where(mine > 0, low, high)
        buffer = join(keep, partner_swap(send, axis, bit, count))
        present.pop(place)
    return buffer


def tree_gather(piece, axis, bits, count):
    me = lax.axis_index(axis)
    present = []
    buffer = piece
    for bit in bits:
        mine = (me >> bit) & 1
        other = partner_swap(buffer, axis, bit, count)
        low = jnp.where(mine > 0, other, buffer)
        high = jnp.where(mine > 0, buffer, other)
        buffer = jnp.stack([low, high], axis=0)
        present.insert(0, bit)
    order = sorted(range(len(present)), key=lambda place: -present[place])
    buffer = jnp.transpose(buffer, order + list(range(len(present), buffer.ndim)))
    return buffer.reshape((count,) + piece.shape)


def add_wide(keep, other):
    return keep.astype(jnp.float32) + other.astype(jnp.float32)


def join_softmax(keep, other):
    width = keep.shape[-1] - 2
    largest = jnp.maximum(keep[..., width], other[..., width])
    factor_keep = jnp.exp(keep[..., width] - largest)
    factor_other = jnp.exp(other[..., width] - largest)
    summed = keep[..., :width] * factor_keep[..., None] + other[..., :width] * factor_other[..., None]
    total = keep[..., width + 1] * factor_keep + other[..., width + 1] * factor_other
    return jnp.concatenate([summed, largest[..., None], total[..., None]], axis=-1)


def rotate(values, positions, head_dim):
    row_count = values.shape[0]
    head_count = values.shape[1] // head_dim
    half_dim = head_dim // 2
    frequency = rotary_base ** (-2.0 * jnp.arange(half_dim, dtype=jnp.float32) / head_dim)
    angles = positions.astype(jnp.float32)[:, None] * frequency[None, :]
    cosine = jnp.cos(angles)[:, None, :]
    sine_part = jnp.sin(angles)[:, None, :]
    shaped = values.reshape(row_count, head_count, head_dim)
    first_half = shaped[:, :, :half_dim]
    second_half = shaped[:, :, half_dim:]
    turned = jnp.concatenate(
        [
            first_half * cosine - second_half * sine_part,
            second_half * cosine + first_half * sine_part,
        ],
        axis=2,
    )
    return turned.reshape(row_count, head_count * head_dim)


def token_layout(prompt_row, prefix_row, row_count):
    run_ends = jnp.cumsum(prompt_row, dtype=jnp.int32)
    starts = run_ends - prompt_row
    offsets = jnp.arange(row_count, dtype=jnp.int32)
    request = jnp.sum(
        (offsets[:, None] >= run_ends[None, :]).astype(jnp.int32), axis=1, dtype=jnp.int32
    )
    member = request[:, None] == jnp.arange(prompt_row.shape[0], dtype=jnp.int32)[None, :]
    start_of = jnp.sum(jnp.where(member, starts[None, :], 0), axis=1, dtype=jnp.int32)
    prefix_of = jnp.sum(jnp.where(member, prefix_row[None, :], 0), axis=1, dtype=jnp.int32)
    return (request, prefix_of + offsets - start_of)


def rescale(summed, factor):
    group_count, row_count, feature_width = summed.shape
    group_size = factor.shape[1]
    shaped = summed.reshape(group_count, row_count, group_size, feature_width // group_size)
    shaped = shaped * jnp.transpose(factor, (0, 2, 1))[:, :, :, None]
    return shaped.reshape(group_count, row_count, feature_width)


def divide_rows(summed, total_weight):
    group_count, row_count, feature_width = summed.shape
    group_size = total_weight.shape[1]
    shaped = summed.reshape(group_count, row_count, group_size, feature_width // group_size)
    shaped = shaped / jnp.transpose(total_weight, (0, 2, 1))[:, :, :, None]
    return shaped.reshape(group_count, row_count, feature_width)


def combine_parts(earlier_part, later_part):
    largest = jnp.maximum(earlier_part[0], later_part[0])
    factor_one = jnp.exp(earlier_part[0] - largest)
    factor_two = jnp.exp(later_part[0] - largest)
    total_weight = earlier_part[1] * factor_one + later_part[1] * factor_two
    summed = rescale(earlier_part[2], factor_one) + rescale(later_part[2], factor_two)
    return (largest, total_weight, summed)


def on_device(
    hidden_in,
    attn_gain,
    qkv_weight,
    out_weight,
    moe_gain,
    router_weight,
    expert_gate,
    expert_up,
    expert_down,
    cache_keys,
    cache_values,
    block_table,
    prefix_lengths,
    prompt_lengths,
    routed_experts,
):
    col_count = lax.axis_size("col")
    row_devices = lax.axis_size("row")
    col_index = lax.axis_index("col")
    row_index = lax.axis_index("row")
    tok_rows = hidden_in.shape[0]
    feature_width = hidden_in.shape[1]
    head_total = out_weight.shape[0]
    head_count = head_total // HEAD_DIM
    key_share = tok_rows // col_count
    request, position = token_layout(prompt_lengths[0], prefix_lengths[0], tok_rows)
    own_start = col_index * key_share
    key_position = lax.dynamic_slice_in_dim(position, own_start, key_share)
    key_request = lax.dynamic_slice_in_dim(request, own_start, key_share)
    residual = hidden_in.astype(jnp.float32)
    squares = jnp.sum(lax.all_gather(jnp.sum(residual * residual, axis=1), "col"), axis=0)
    scale_one = lax.rsqrt(squares / D + norm_epsilon)
    normed = (residual * scale_one[:, None] * attn_gain[None, :]).astype(jnp.bfloat16)
    scatter_bits = [0] + list(range(1, col_count.bit_length() - 1))
    gather_bits = scatter_bits[::-1]
    query_part = jnp.dot(normed, qkv_weight[:, :head_total], preferred_element_type=jnp.float32)
    kv_part = jnp.dot(
        normed, qkv_weight[:, head_total:], preferred_element_type=jnp.float32
    ).astype(jnp.bfloat16)
    both_part = jnp.concatenate([query_part, kv_part.astype(jnp.float32)], axis=1)
    both_sum = tree_scatter(
        both_part.reshape(col_count, key_share, both_part.shape[1]), "col", scatter_bits, add_wide
    )
    own_queries = (
        rotate(both_sum[:, :head_total], key_position, HEAD_DIM) * HEAD_DIM ** (-0.5)
    ).astype(jnp.bfloat16)
    queries = tree_gather(own_queries, "col", gather_bits, col_count).reshape(
        tok_rows, head_total
    )
    key_value = both_sum[:, head_total:]
    new_keys = rotate(key_value[:, :head_total], key_position, HEAD_DIM).astype(jnp.bfloat16)
    new_values = key_value[:, head_total:].astype(jnp.bfloat16)
    pool_size = cache_keys.shape[0]
    page_size = cache_keys.shape[1]
    req_count = block_table.shape[1]
    pages_each = block_table.shape[2] // col_count
    page_table = block_table[0].reshape(req_count, pages_each, col_count)
    own_pages = lax.dynamic_slice_in_dim(page_table, col_index, 1, 2).reshape(
        req_count * pages_each
    )
    pool_offset_begin = (row_index * col_count + col_index) * pool_size
    slot_ids = jnp.arange(pool_size, dtype=jnp.int32)
    entry_ids = jnp.arange(req_count * pages_each, dtype=jnp.int32)
    slot_match = (own_pages - pool_offset_begin)[None, :] == slot_ids[:, None]
    entry_request = entry_ids // pages_each
    entry_page = entry_ids % pages_each * col_count + col_index
    slot_request = jnp.sum(
        jnp.where(slot_match, entry_request[None, :], 0), axis=1, dtype=jnp.int32
    )
    slot_page = jnp.sum(jnp.where(slot_match, entry_page[None, :], 0), axis=1, dtype=jnp.int32)
    prefix_row = prefix_lengths[0]
    slot_prefix = jnp.sum(
        jnp.where(
            slot_request[:, None] == jnp.arange(req_count, dtype=jnp.int32)[None, :],
            prefix_row[None, :],
            0,
        ),
        axis=1,
        dtype=jnp.int32,
    )
    cache_position = (
        slot_page[:, None] * page_size + jnp.arange(page_size, dtype=jnp.int32)[None, :]
    )
    cache_live = (
        (cache_position < slot_prefix[:, None]).astype(jnp.int32).reshape(pool_size * page_size)
    )
    cache_request = jnp.broadcast_to(slot_request[:, None], (pool_size, page_size)).reshape(
        pool_size * page_size
    )
    cache_mask = (request[:, None] == cache_request[None, :]) & (cache_live[None, :] > 0)
    fresh_mask = (request[:, None] == key_request[None, :]) & (
        key_position[None, :] <= position[:, None]
    )
    query_heads = queries.reshape(tok_rows, head_count, HEAD_DIM)
    key_heads = jnp.concatenate(
        [cache_keys.reshape(pool_size * page_size, head_total), new_keys], axis=0
    ).reshape(pool_size * page_size + key_share, head_count, HEAD_DIM)
    value_heads = jnp.concatenate(
        [cache_values.reshape(pool_size * page_size, head_total), new_values], axis=0
    ).reshape(pool_size * page_size + key_share, head_count, HEAD_DIM)
    key_mask = jnp.concatenate([cache_mask, fresh_mask], axis=1)
    score_matrix = jnp.einsum(
        "thd,khd->htk", query_heads, key_heads, preferred_element_type=jnp.float32
    )
    score_matrix = jnp.where(key_mask[None], score_matrix, masked_score)
    local_max = jnp.max(score_matrix, axis=2)
    weights = jnp.where(key_mask[None], jnp.exp(score_matrix - local_max[:, :, None]), 0.0)
    local_total = jnp.sum(weights, axis=2)
    local_sum = jnp.einsum(
        "htk,khd->thd",
        weights.astype(jnp.bfloat16),
        value_heads,
        preferred_element_type=jnp.float32,
    )
    packed = jnp.concatenate(
        [
            local_sum,
            jnp.transpose(local_max)[:, :, None],
            jnp.transpose(local_total)[:, :, None],
        ],
        axis=2,
    )
    merged_rows = tree_scatter(
        packed.reshape((col_count, key_share) + packed.shape[1:]), "col", scatter_bits, join_softmax
    )
    own_attended = (
        merged_rows[..., :HEAD_DIM] / merged_rows[..., HEAD_DIM + 1][..., None]
    ).reshape(key_share, head_total).astype(jnp.bfloat16)
    attended = tree_gather(own_attended, "col", gather_bits, col_count).reshape(
        tok_rows, head_total
    )
    projected = jnp.dot(attended, out_weight, preferred_element_type=jnp.float32)
    attn_out = projected.astype(jnp.bfloat16)
    middle = (residual + residual_scale * attn_out.astype(jnp.float32)).astype(jnp.bfloat16)
    middle_wide = middle.astype(jnp.float32)
    router_part = jnp.dot(
        middle_wide * moe_gain[None, :], router_weight, precision=lax.Precision.HIGHEST
    )
    stats = jnp.sum(
        lax.all_gather(
            jnp.concatenate(
                [jnp.sum(middle_wide * middle_wide, axis=1, keepdims=True), router_part], axis=1
            ),
            "col",
        ),
        axis=0,
    )
    scale_two = lax.rsqrt(stats[:, 0] / D + norm_epsilon)
    moe_normed_f = middle_wide * scale_two[:, None] * moe_gain[None, :]
    logits = stats[:, 1:] * scale_two[:, None]
    moe_normed = moe_normed_f.astype(jnp.bfloat16)
    expert_local = expert_gate.shape[0]
    expert_total = expert_local * row_devices
    capacity = 2 * TOP * tok_rows // expert_total
    onehot_three = (
        routed_experts[:, :, None] == jnp.arange(expert_total, dtype=jnp.int32)[None, None, :]
    )
    selected_logits = jnp.sum(jnp.where(onehot_three, logits[:, None, :], 0.0), axis=2)
    first_gate = jax.nn.sigmoid(selected_logits[:, 0] - selected_logits[:, 1])
    gate_pair = jnp.stack([first_gate, 1.0 - first_gate], axis=1)
    onehot = onehot_three.astype(jnp.int32).reshape(tok_rows * TOP, expert_total)
    earlier = jnp.cumsum(onehot, axis=0, dtype=jnp.int32) - onehot
    slot_index = jnp.sum(earlier * onehot, axis=1, dtype=jnp.int32)
    target = routed_experts.reshape(tok_rows * TOP) * capacity + slot_index
    token_local = jnp.arange(tok_rows * TOP, dtype=jnp.int32) // TOP
    source = jnp.zeros((expert_total * capacity,), jnp.int32).at[target].set(token_local)
    filled = jnp.zeros((expert_total * capacity,), jnp.int32).at[target].set(1)
    outgoing = jnp.where(
        filled[:, None] > 0, moe_normed[source], jnp.zeros((), jnp.bfloat16)
    ).reshape(expert_total, capacity, feature_width)
    arrived = lax.all_to_all(outgoing, "row", split_axis=0, concat_axis=0, tiled=True)
    expert_rows = (
        arrived.reshape(row_devices, expert_local, capacity, feature_width)
        .transpose(1, 0, 2, 3)
        .reshape(expert_local, row_devices * capacity, feature_width)
    )
    gathered = tree_gather(
        jnp.transpose(expert_rows, (0, 2, 1)), "col", gather_bits, col_count
    )
    feature_piece = jnp.transpose(gathered, (1, 0, 2, 3)).reshape(
        expert_local, col_count * feature_width, gathered.shape[3]
    )
    gate_next = jnp.einsum(
        "edr,edf->erf", feature_piece, expert_gate, preferred_element_type=jnp.float32
    )
    up_next = jnp.einsum(
        "edr,edf->erf", feature_piece, expert_up, preferred_element_type=jnp.float32
    )
    hidden = (jax.nn.silu(gate_next) * up_next).astype(jnp.bfloat16)
    received_rows = hidden.shape[1]
    value_partial_sum = jnp.einsum(
        "efo,erf->oer", expert_down, hidden, preferred_element_type=jnp.float32
    )
    expert_out = tree_scatter(
        value_partial_sum.reshape(
            col_count, feature_width, expert_local * received_rows
        ).astype(jnp.bfloat16),
        "col",
        scatter_bits,
        add_wide,
    ).astype(jnp.bfloat16)
    returned = lax.all_to_all(
        expert_out.reshape(feature_width, expert_local, received_rows),
        "row",
        split_axis=2,
        concat_axis=1,
        tiled=True,
    )
    flat_back = returned.reshape(feature_width, expert_total * capacity)
    picked = (
        jnp.take(flat_back, target, axis=1)
        .astype(jnp.float32)
        .reshape(feature_width, tok_rows, TOP)
    )
    moe_columns = jnp.sum(picked * gate_pair[None, :, :], axis=2).astype(jnp.bfloat16)
    moe_out = moe_columns.T
    layer_out = (middle_wide + residual_scale * moe_out.astype(jnp.float32)).astype(jnp.bfloat16)
    return (attn_out, moe_out, layer_out)


def solution(mesh):
    in_specs = (
        P("row", "col"),
        P("col"),
        P("col", None),
        P(None, "col"),
        P("col"),
        P("col", None),
        P("row", None, "col"),
        P("row", None, "col"),
        P("row", "col", None),
        P(("row", "col"), None, None),
        P(("row", "col"), None, None),
        P("row", None, None),
        P("row", None),
        P("row", None),
        P("row", None),
    )
    out_specs = (P("row", "col"), P("row", "col"), P("row", "col"))
    return jax.shard_map(
        on_device, mesh=mesh, in_specs=in_specs, out_specs=out_specs, check_vma=False
    )
```
